128 devices in a mesh: grp: 4 (over z), dev: 32 (over x, y, core).
Axes of the slice: x: 4, y: 4, z: 4, core: 2. Of those that a mesh axis runs over, the one named last changes fastest.
Arguments:
- packed_w: bfloat16 [4, 8192, 8192], P(None, 'dev', 'grp'), may hold values from -0.0625 to 0.0625
- packed_t: bfloat16 [4, 8192, 1536], P(None, 'dev', 'grp'), may hold values from -6 to 6
- row_energy: float32 [4, 8192], P('grp', 'dev'), may hold values from 0.3 to 4
- col_energy: float32 [4, 1536], P('grp'), may hold values from 0.3 to 4
- block_order: int32 [4], replicated, may hold values from 3072 to 8192, as said below
Outputs:
- new_amps: float32 [4, 8192, 1536], P(None, 'dev', 'grp')
The draws below stay inside these ranges and needn't reach their ends.
Inputs may be any that keep to these rules, and one draw needn't show every extreme that they name: `block_order`: one block has order exactly 8192; the others lie between 3072 and 8191.
All inputs are finite; a program needn't handle non-finite values.
Results may differ from the reference program's by a relative error of at most 0.0003.
Values may be sent and summed in bfloat16 or wider, within the bound.
No kernel may reach another device: no remote copies, remote signals or barrier semaphores. Data moves between devices by JAX's collectives and lax.ppermute only.
A program may use at most 192 MiB of HBM per device.

```python
import math
import jax
import jax.numpy as jnp
from jax import lax

BLOCKS = 4
ORDER_MAX = 8192
COLS = 1536
N_DEV = 32


def draw_block_order(key, part):
    first, second = jax.random.split(jax.random.fold_in(key, 11))
    base = jax.random.randint(first, (BLOCKS,), ORDER_MAX * 3 // 8, ORDER_MAX)
    chosen = jax.random.randint(second, (), 0, BLOCKS)
    return jnp.where(jnp.arange(BLOCKS) == chosen, ORDER_MAX, base).astype(jnp.int32)


def steps_of(key, dims, cuts, smallest, high):
    level = 1.0
    for dim, shards_of in cuts:
        heights = jax.random.uniform(jax.random.fold_in(jax.random.fold_in(key, 6), dim), (shards_of,), jnp.float32, smallest / len(cuts), high / len(cuts))
        level = level * jnp.repeat(jnp.exp(heights), dims[dim] // shards_of).reshape((-1,) + (1,) * (len(dims) - 1 - dim))
    return level


def noise(own_key, dims, scale, most, cuts=(), kind=jnp.bfloat16):
    factor_of = steps_of(own_key, dims, cuts, -0.22, 0.18) if cuts else 1.0
    result = jax.random.normal(own_key, dims, jnp.float32) * scale * factor_of
    return jnp.minimum(jnp.maximum(result, -most), most).astype(kind)


def setup_inputs(seed: int = 0) -> dict:
    seeds = jax.random.split(jax.random.key(seed), 6)
    packed_w = noise(seeds[0], (BLOCKS, ORDER_MAX, ORDER_MAX), ORDER_MAX ** -0.5, 0.0625, ((1, 32), (2, 4)))
    packed_t = noise(seeds[1], (BLOCKS, ORDER_MAX, COLS), 1.0, 6.0, ((1, 32), (2, 4)))
    row_energy = jnp.clip(jnp.exp(math.log(4.0) - 2.5902671 * jax.random.uniform(seeds[2], (BLOCKS, ORDER_MAX), jnp.float32) ** steps_of(seeds[2], (BLOCKS, ORDER_MAX), ((0, 4), (1, 32)), -0.2, 0.2)), 0.3, 4.0)
    col_energy = jnp.clip(jnp.exp(math.log(4.0) - 2.5902671 * jax.random.uniform(seeds[3], (BLOCKS, COLS), jnp.float32) ** steps_of(seeds[3], (BLOCKS, COLS), ((0, 4),), -0.2, 0.2)), 0.3, 4.0)
    block_order = draw_block_order(jax.random.fold_in(seeds[5], 71), 0)
    return {"packed_w": packed_w, "packed_t": packed_t, "row_energy": row_energy, "col_energy": col_energy, "block_order": block_order}


def reference(packed_w, packed_t, row_energy, col_energy, block_order):
    rows_dev = ORDER_MAX // N_DEV
    index = jnp.arange(ORDER_MAX, dtype=jnp.int32)
    true_rows = (index % rows_dev) * N_DEV + index // rows_dev
    results = []
    for block in range(BLOCKS):
        live = true_rows < block_order[block]
        amps = packed_t[block]
        masked = jnp.where(live[:, None], amps, jnp.zeros_like(amps))
        cycle = jnp.dot(packed_w[block].astype(jnp.float32), masked.astype(jnp.float32), precision=lax.Precision.HIGHEST)
        denom = row_energy[block][:, None] + col_energy[block][None, :]
        update = jnp.where(live[:, None], cycle / denom, jnp.zeros_like(cycle))
        results.append(amps.astype(jnp.float32) + update)
    return jnp.stack(results, axis=0)
```

```python
import jax
import jax.numpy as jnp
from jax import lax
from jax.sharding import Mesh, NamedSharding, PartitionSpec as P


def apply_update(t_rows, cycle, live, row_gap, col_gap):
    denom = row_gap[:, None] + col_gap[None, :]
    update = jnp.where(live[:, None], cycle / denom, jnp.zeros_like(cycle))
    return t_rows.astype(jnp.float32) + update


def shards(packed_w, packed_t, row_energy, col_energy, block_order):
    nchip = lax.axis_size("chip")
    ncore = lax.axis_size("dc")
    rank = lax.axis_index("chip") * ncore + lax.axis_index("dc")
    group = lax.axis_index("grp")
    local = packed_t.shape[1]
    ndev = nchip * ncore
    true_rows = jnp.arange(local, dtype=jnp.int32) * ndev + rank
    t_rows = lax.all_to_all(packed_t, "grp", split_axis=0, concat_axis=2, tiled=True)[0]
    order = lax.dynamic_index_in_dim(block_order, group, 0, keepdims=False)
    live = true_rows < order
    t_live = jnp.where(live[:, None], t_rows, jnp.zeros_like(t_rows))
    t_half = lax.all_gather(t_live, "chip", axis=0, tiled=True)
    w_rows = lax.all_to_all(packed_w, "grp", split_axis=0, concat_axis=2, tiled=True)[0]
    w4 = w_rows.reshape(local, nchip, ncore, local)
    w_mine = lax.all_to_all(w4, "dc", split_axis=2, concat_axis=0, tiled=True)
    w_mine = w_mine.reshape(ncore * local, nchip * local)
    partial = jnp.dot(w_mine, t_half, preferred_element_type=jnp.float32)
    cycle = lax.psum_scatter(partial, "dc", scatter_dimension=0, tiled=True)
    new_block = apply_update(t_rows, cycle, live, row_energy[0], col_energy[0])
    return lax.all_to_all(new_block[None], "grp", split_axis=2, concat_axis=0, tiled=True)


def solution(mesh):
    ngrp, ndev = mesh.devices.shape
    ncore = 2
    split = Mesh(mesh.devices.reshape(ngrp, ndev // ncore, ncore), ("grp", "chip", "dc"))
    rows = ("chip", "dc")
    in_specs = (P(None, rows, "grp"), P(None, rows, "grp"), P("grp", rows), P("grp", None), P())
    out_specs = P(None, rows, "grp")
    body = jax.shard_map(shards, mesh=split, in_specs=in_specs, out_specs=out_specs, check_vma=False)
    target = NamedSharding(mesh, P(None, "dev", "grp"))

    def run(*args):
        return lax.with_sharding_constraint(body(*args), target)

    return run
```

```python
import jax
import jax.numpy as jnp
from jax import lax
from jax.sharding import Mesh, NamedSharding, PartitionSpec as P


def apply_update(t_rows, cycle, live, row_gap, col_gap):
    denom = row_gap[:, None] + col_gap[None, :]
    update = jnp.where(live[:, None], cycle / denom, jnp.zeros_like(cycle))
    return t_rows.astype(jnp.float32) + update


def shift(x, axis, step):
    n = lax.axis_size(axis)
    return lax.ppermute(x, axis, [(i, (i + step) % n) for i in range(n)])


def ring4(x, axis):
    from_left = shift(x, axis, 1)
    from_right = shift(x, axis, -1)
    half = x.shape[0] // 2
    far_lo = shift(from_left[:half], axis, 1)
    far_hi = shift(from_right[half:], axis, -1)
    far = jnp.concatenate([far_lo, far_hi], axis=0)
    return jnp.stack([x, from_right, far, from_left], axis=0)


def shards(packed_w, packed_t, row_energy, col_energy, block_order):
    nx = lax.axis_size("dx")
    ny = lax.axis_size("dy")
    ncore = lax.axis_size("dc")
    ngrp = lax.axis_size("grp")
    x = lax.axis_index("dx")
    y = lax.axis_index("dy")
    c = lax.axis_index("dc")
    z = lax.axis_index("grp")
    rank = (x * ny + y) * ncore + c
    local = packed_t.shape[1]
    ndev = nx * ny * ncore
    true_rows = jnp.arange(local, dtype=jnp.int32) * ndev + rank

    t_rows = lax.all_to_all(packed_t, "grp", split_axis=0, concat_axis=2, tiled=True)[0]
    order = lax.dynamic_index_in_dim(block_order, z, 0, keepdims=False)
    live = true_rows < order
    t_live = jnp.where(live[:, None], t_rows, jnp.zeros_like(t_rows))

    half = local // 2
    col_a = ring4(t_live[:half], "dy")
    row_b = ring4(t_live[half:], "dx")
    all_a = ring4(col_a, "dx")
    all_b = ring4(row_b, "dy")

    cols = packed_w.shape[2] // (ny * ncore)
    w5 = packed_w.reshape(ngrp, local, ny, ncore, cols)
    w_c = lax.all_to_all(w5, "dc", split_axis=3, concat_axis=1, tiled=True)
    w_c = w_c.reshape(ngrp, ncore * local, ny, cols)
    got = [lax.dynamic_index_in_dim(w_c, z, 0, keepdims=False)]
    for s in range(1, ngrp):
        part = lax.dynamic_index_in_dim(w_c, (z + s) % ngrp, 0, keepdims=False)
        got.append(shift(part, "grp", s))
    w_s = jnp.stack(got, axis=0)
    ox = jnp.arange(nx, dtype=jnp.int32)
    oy = jnp.arange(ny, dtype=jnp.int32)
    s_of = (z - x - ox) % ngrp
    y_of = (y + oy) % ny
    w_rel = w_s[s_of][:, :, y_of]
    w_a = jnp.transpose(w_rel[..., :half], (1, 0, 2, 3)).reshape(ncore * local, -1)
    w_b = jnp.transpose(w_rel[..., half:], (1, 2, 0, 3)).reshape(ncore * local, -1)
    ncol = t_live.shape[1]
    partial = jnp.dot(w_a, all_a.reshape(-1, ncol), preferred_element_type=jnp.float32)
    partial = partial + jnp.dot(w_b, all_b.reshape(-1, ncol), preferred_element_type=jnp.float32)

    other = lax.dynamic_slice_in_dim(partial, (1 - c) * local, local, 0)
    mine = lax.dynamic_slice_in_dim(partial, c * local, local, 0)
    cycle = mine + shift(other, "dc", 1)
    new_block = apply_update(t_rows, cycle, live, row_energy[0], col_energy[0])
    return lax.all_to_all(new_block[None], "grp", split_axis=2, concat_axis=0, tiled=True)


def solution(mesh):
    ngrp, ndev = mesh.devices.shape
    ncore = 2
    nx = 4
    ny = ndev // (ncore * nx)
    split = Mesh(mesh.devices.reshape(ngrp, nx, ny, ncore), ("grp", "dx", "dy", "dc"))
    rows = ("dx", "dy", "dc")
    in_specs = (P(None, rows, "grp"), P(None, rows, "grp"), P("grp", rows), P("grp", None), P())
    out_specs = P(None, rows, "grp")
    body = jax.shard_map(shards, mesh=split, in_specs=in_specs, out_specs=out_specs, check_vma=False)
    target = NamedSharding(mesh, P(None, "dev", "grp"))

    def run(*args):
        return lax.with_sharding_constraint(body(*args), target)

    return run
```

```python
import jax
import jax.numpy as jnp
from jax import lax
from jax.sharding import Mesh, NamedSharding, PartitionSpec as P


def apply_update(t_rows, cycle, live, row_gap, col_gap):
    denom = row_gap[:, None] + col_gap[None, :]
    update = jnp.where(live[:, None], cycle / denom, jnp.zeros_like(cycle))
    return t_rows.astype(jnp.float32) + update


def shift(x, axis, step):
    n = lax.axis_size(axis)
    return lax.ppermute(x, axis, [(i, (i + step) % n) for i in range(n)])


def place(buf, piece, index, axis):
    start = [0] * buf.ndim
    start[axis] = index
    return lax.dynamic_update_slice(buf, jnp.expand_dims(piece, axis), start)


def ring4(x, axis, me, buf, buf_axis):
    n = lax.axis_size(axis)
    from_left = shift(x, axis, 1)
    from_right = shift(x, axis, -1)
    half = x.shape[0] // 2
    far_lo = shift(from_left[:half], axis, 1)
    far_hi = shift(from_right[half:], axis, -1)
    buf = place(buf, x, me, buf_axis)
    buf = place(buf, from_left, (me + n - 1) % n, buf_axis)
    buf = place(buf, from_right, (me + 1) % n, buf_axis)
    far = (me + 2) % n
    lo = [0] * buf.ndim
    lo[buf_axis] = far
    buf = lax.dynamic_update_slice(buf, jnp.expand_dims(far_lo, buf_axis), lo)
    hi = list(lo)
    hi[buf_axis + 1] = half
    buf = lax.dynamic_update_slice(buf, jnp.expand_dims(far_hi, buf_axis), hi)
    return buf


def shards(packed_w, packed_t, row_energy, col_energy, block_order):
    nx = lax.axis_size("dx")
    ny = lax.axis_size("dy")
    ncore = lax.axis_size("dc")
    ngrp = lax.axis_size("grp")
    x = lax.axis_index("dx")
    y = lax.axis_index("dy")
    c = lax.axis_index("dc")
    z = lax.axis_index("grp")
    rank = (x * ny + y) * ncore + c
    local = packed_t.shape[1]
    ndev = nx * ny * ncore
    true_rows = jnp.arange(local, dtype=jnp.int32) * ndev + rank

    t_rows = lax.all_to_all(packed_t, "grp", split_axis=0, concat_axis=2, tiled=True)[0]
    order = lax.dynamic_index_in_dim(block_order, z, 0, keepdims=False)
    live = true_rows < order
    t_live = jnp.where(live[:, None], t_rows, jnp.zeros_like(t_rows))
    ncol = t_live.shape[1]

    half = local // 2
    col_a = ring4(t_live[:half], "dy", y, jnp.zeros((ny, half, ncol), t_live.dtype), 0)
    row_b = ring4(t_live[half:], "dx", x, jnp.zeros((nx, half, ncol), t_live.dtype), 0)
    t_abs = jnp.zeros((nx, ny, local, ncol), t_live.dtype)
    t_abs = ring4(col_a, "dx", x, t_abs[:, :, :half], 0)
    t_b = ring4(row_b, "dy", y, jnp.zeros((ny, nx, half, ncol), t_live.dtype), 0)
    t_abs = jnp.concatenate([t_abs, jnp.transpose(t_b, (1, 0, 2, 3))], axis=2)

    cols = packed_w.shape[2] // (ny * ncore)
    wv = packed_w.reshape(ngrp, local, ny, ncore, cols)
    w_own = jnp.zeros((local, nx, ny, cols), packed_w.dtype)
    w_oth = jnp.zeros((local, nx, ny, cols), packed_w.dtype)
    for sz in range(ngrp):
        for sc in range(ncore):
            piece = wv[(z + sz) % ngrp, :, :, (c + sc) % ncore, :]
            if sz or sc:
                n = ngrp * ncore
                perm = []
                for i in range(n):
                    gi, ci = divmod(i, ncore)
                    perm.append((i, ((gi + sz) % ngrp) * ncore + (ci + sc) % ncore))
                piece = lax.ppermute(piece, ("grp", "dc"), perm)
            where = (z - sz) % ngrp
            if sc:
                w_oth = place(w_oth, piece, where, 1)
            else:
                w_own = place(w_own, piece, where, 1)

    t_flat = t_abs.reshape(-1, ncol)
    mine = jnp.dot(w_own.reshape(local, -1), t_flat, preferred_element_type=jnp.float32)
    other = jnp.dot(w_oth.reshape(local, -1), t_flat, preferred_element_type=jnp.float32)
    cycle = mine + shift(other, "dc", 1)
    new_block = apply_update(t_rows, cycle, live, row_energy[0], col_energy[0])
    return lax.all_to_all(new_block[None], "grp", split_axis=2, concat_axis=0, tiled=True)


def solution(mesh):
    ngrp, ndev = mesh.devices.shape
    ncore = 2
    nx = 4
    ny = ndev // (ncore * nx)
    split = Mesh(mesh.devices.reshape(ngrp, nx, ny, ncore), ("grp", "dx", "dy", "dc"))
    rows = ("dx", "dy", "dc")
    in_specs = (P(None, rows, "grp"), P(None, rows, "grp"), P("grp", rows), P("grp", None), P())
    out_specs = P(None, rows, "grp")
    body = jax.shard_map(shards, mesh=split, in_specs=in_specs, out_specs=out_specs, check_vma=False)
    target = NamedSharding(mesh, P(None, "dev", "grp"))

    def run(*args):
        return lax.with_sharding_constraint(body(*args), target)

    return run
```

```python
import jax
import jax.numpy as jnp
from jax import lax
from jax.sharding import Mesh, NamedSharding, PartitionSpec as P


def apply_update(t_rows, cycle, live, row_gap, col_gap):
    denom = row_gap[:, None] + col_gap[None, :]
    update = jnp.where(live[:, None], cycle / denom, jnp.zeros_like(cycle))
    return t_rows.astype(jnp.float32) + update


def shift(x, axis, step):
    n = lax.axis_size(axis)
    return lax.ppermute(x, axis, [(i, (i + step) % n) for i in range(n)])


def put(buf, piece, base, axis, index):
    start = list(base)
    start[axis] = index
    return lax.dynamic_update_slice(buf, jnp.expand_dims(piece, axis), start)


def ring4(x, axis, me, buf, buf_axis, base):
    n = lax.axis_size(axis)
    from_left = shift(x, axis, 1)
    from_right = shift(x, axis, -1)
    half = x.shape[0] // 2
    far_lo = shift(from_left[:half], axis, 1)
    far_hi = shift(from_right[half:], axis, -1)
    buf = put(buf, x, base, buf_axis, me)
    buf = put(buf, from_left, base, buf_axis, (me + n - 1) % n)
    buf = put(buf, from_right, base, buf_axis, (me + 1) % n)
    far = (me + 2) % n
    buf = put(buf, far_lo, base, buf_axis, far)
    hi = list(base)
    inner = buf_axis + 1 if buf_axis == 0 else 0
    hi[inner] = hi[inner] + half
    buf = put(buf, far_hi, hi, buf_axis, far)
    return buf


def shards(packed_w, packed_t, row_energy, col_energy, block_order):
    nx = lax.axis_size("dx")
    ny = lax.axis_size("dy")
    ncore = lax.axis_size("dc")
    ngrp = lax.axis_size("grp")
    x = lax.axis_index("dx")
    y = lax.axis_index("dy")
    c = lax.axis_index("dc")
    z = lax.axis_index("grp")
    rank = (x * ny + y) * ncore + c
    local = packed_t.shape[1]
    ndev = nx * ny * ncore
    true_rows = jnp.arange(local, dtype=jnp.int32) * ndev + rank

    t_rows = lax.all_to_all(packed_t, "grp", split_axis=0, concat_axis=2, tiled=True)[0]
    order = lax.dynamic_index_in_dim(block_order, z, 0, keepdims=False)
    live = true_rows < order
    t_live = jnp.where(live[:, None], t_rows, jnp.zeros_like(t_rows))
    ncol = t_live.shape[1]

    half = local // 2
    col_a = ring4(t_live[:half], "dy", y, jnp.zeros((ny, half, ncol), t_live.dtype), 0, (0, 0, 0))
    row_b = ring4(t_live[half:], "dx", x, jnp.zeros((nx, half, ncol), t_live.dtype), 0, (0, 0, 0))
    t_abs = jnp.zeros((nx, ny, local, ncol), t_live.dtype)
    t_abs = ring4(col_a, "dx", x, t_abs, 0, (0, 0, 0, 0))
    t_abs = ring4(row_b, "dy", y, t_abs, 1, (0, 0, half, 0))

    span = packed_w.shape[2] // ny
    cols = span // ncore
    w_own = jnp.zeros((local, nx * ny * cols), packed_w.dtype)
    w_oth = jnp.zeros((local, nx * ny * cols), packed_w.dtype)
    for sz in range(ngrp):
        for sc in range(ncore):
            zt = (z + sz) % ngrp
            ct = (c + sc) % ncore
            piece = jnp.concatenate(
                [lax.dynamic_slice(packed_w, (zt, 0, j * span + ct * cols), (1, local, cols))[0]
                 for j in range(ny)], axis=1)
            if sz or sc:
                n = ngrp * ncore
                perm = []
                for i in range(n):
                    gi, ci = divmod(i, ncore)
                    perm.append((i, ((gi + sz) % ngrp) * ncore + (ci + sc) % ncore))
                piece = lax.ppermute(piece, ("grp", "dc"), perm)
            where = ((z - sz) % ngrp) * (ny * cols)
            if sc:
                w_oth = lax.dynamic_update_slice(w_oth, piece, (0, where))
            else:
                w_own = lax.dynamic_update_slice(w_own, piece, (0, where))

    t_flat = t_abs.reshape(-1, ncol)
    mine = jnp.dot(w_own, t_flat, preferred_element_type=jnp.float32)
    other = jnp.dot(w_oth, t_flat, preferred_element_type=jnp.float32)
    cycle = mine + shift(other, "dc", 1)
    new_block = apply_update(t_rows, cycle, live, row_energy[0], col_energy[0])
    return lax.all_to_all(new_block[None], "grp", split_axis=2, concat_axis=0, tiled=True)


def solution(mesh):
    ngrp, ndev = mesh.devices.shape
    ncore = 2
    nx = 4
    ny = ndev // (ncore * nx)
    split = Mesh(mesh.devices.reshape(ngrp, nx, ny, ncore), ("grp", "dx", "dy", "dc"))
    rows = ("dx", "dy", "dc")
    in_specs = (P(None, rows, "grp"), P(None, rows, "grp"), P("grp", rows), P("grp", None), P())
    out_specs = P(None, rows, "grp")
    body = jax.shard_map(shards, mesh=split, in_specs=in_specs, out_specs=out_specs, check_vma=False)
    target = NamedSharding(mesh, P(None, "dev", "grp"))

    def run(*args):
        return lax.with_sharding_constraint(body(*args), target)

    return run
```

```python
import jax
import jax.numpy as jnp
from jax import lax
from jax.sharding import Mesh, NamedSharding, PartitionSpec as P


def apply_update(t_rows, cycle, live, row_gap, col_gap):
    denom = row_gap[:, None] + col_gap[None, :]
    update = jnp.where(live[:, None], cycle / denom, jnp.zeros_like(cycle))
    return t_rows.astype(jnp.float32) + update


def shift(x, axis, step):
    n = lax.axis_size(axis)
    return lax.ppermute(x, axis, [(i, (i + step) % n) for i in range(n)])


def ring4(x, axis):
    from_left = shift(x, axis, 1)
    from_right = shift(x, axis, -1)
    half = x.shape[0] // 2
    far_lo = shift(from_left[:half], axis, 1)
    far_hi = shift(from_right[half:], axis, -1)
    far = jnp.concatenate([far_lo, far_hi], axis=0)
    return jnp.stack([x, from_right, far, from_left], axis=0)


def shards(packed_w, packed_t, row_energy, col_energy, block_order):
    nx = lax.axis_size("dx")
    ny = lax.axis_size("dy")
    ncore = lax.axis_size("dc")
    ngrp = lax.axis_size("grp")
    x = lax.axis_index("dx")
    y = lax.axis_index("dy")
    c = lax.axis_index("dc")
    z = lax.axis_index("grp")
    rank = (x * ny + y) * ncore + c
    local = packed_t.shape[1]
    ndev = nx * ny * ncore
    true_rows = jnp.arange(local, dtype=jnp.int32) * ndev + rank

    t_rows = lax.all_to_all(packed_t, "grp", split_axis=0, concat_axis=2, tiled=True)[0]
    order = lax.dynamic_index_in_dim(block_order, z, 0, keepdims=False)
    live = true_rows < order
    t_live = jnp.where(live[:, None], t_rows, jnp.zeros_like(t_rows))
    ncol = t_live.shape[1]

    half = local // 2
    t_a = ring4(ring4(t_live[:half], "dy"), "dx").reshape(-1, ncol)
    t_b = ring4(ring4(t_live[half:], "dx"), "dy").reshape(-1, ncol)

    span = packed_w.shape[2] // ny
    cols = span // ncore
    w_a = jnp.zeros((ncore * local, nx * ny * half), packed_w.dtype)
    w_b = jnp.zeros((ncore * local, nx * ny * half), packed_w.dtype)
    for sz in range(ngrp):
        for sc in range(ncore):
            zt = (z + sz) % ngrp
            ct = (c + sc) % ncore
            parts = []
            for lo in (0, half):
                for oy in range(ny):
                    at = ((y + oy) % ny) * span + ct * cols + lo
                    parts.append(lax.dynamic_slice(packed_w, (zt, 0, at), (1, local, half))[0])
            piece = jnp.concatenate(parts, axis=1)
            if sz or sc:
                n = ngrp * ncore
                perm = []
                for i in range(n):
                    gi, ci = divmod(i, ncore)
                    perm.append((i, ((gi + sz) % ngrp) * ncore + (ci + sc) % ncore))
                piece = lax.ppermute(piece, ("grp", "dc"), perm)
            ox = (z - sz - x) % nx
            r0 = sc * local
            w_a = lax.dynamic_update_slice(w_a, piece[:, :ny * half], (r0, ox * ny * half))
            for oy in range(ny):
                part = piece[:, (ny + oy) * half:(ny + oy + 1) * half]
                w_b = lax.dynamic_update_slice(w_b, part, (r0, oy * nx * half + ox * half))

    partial = jnp.dot(w_a, t_a, preferred_element_type=jnp.float32)
    partial = partial + jnp.dot(w_b, t_b, preferred_element_type=jnp.float32)
    mine = partial[:local]
    other = partial[local:]
    cycle = mine + shift(other, "dc", 1)
    new_block = apply_update(t_rows, cycle, live, row_energy[0], col_energy[0])
    return lax.all_to_all(new_block[None], "grp", split_axis=2, concat_axis=0, tiled=True)


def solution(mesh):
    ngrp, ndev = mesh.devices.shape
    ncore = 2
    nx = 4
    ny = ndev // (ncore * nx)
    split = Mesh(mesh.devices.reshape(ngrp, nx, ny, ncore), ("grp", "dx", "dy", "dc"))
    rows = ("dx", "dy", "dc")
    in_specs = (P(None, rows, "grp"), P(None, rows, "grp"), P("grp", rows), P("grp", None), P())
    out_specs = P(None, rows, "grp")
    body = jax.shard_map(shards, mesh=split, in_specs=in_specs, out_specs=out_specs, check_vma=False)
    target = NamedSharding(mesh, P(None, "dev", "grp"))

    def run(*args):
        return lax.with_sharding_constraint(body(*args), target)

    return run
```

```python
import jax
import jax.numpy as jnp
from jax import lax
from jax.sharding import Mesh, NamedSharding, PartitionSpec as P


def apply_update(t_rows, cycle, live, row_gap, col_gap):
    denom = row_gap[:, None] + col_gap[None, :]
    update = jnp.where(live[:, None], cycle / denom, jnp.zeros_like(cycle))
    return t_rows.astype(jnp.float32) + update


def shift(x, axis, step):
    n = lax.axis_size(axis)
    return lax.ppermute(x, axis, [(i, (i + step) % n) for i in range(n)])


def put(buf, piece, base, axis, index):
    start = list(base)
    start[axis] = index
    return lax.dynamic_update_slice(buf, jnp.expand_dims(piece, axis), start)


def ring4(x, axis, me, buf, buf_axis, base):
    n = lax.axis_size(axis)
    from_left = shift(x, axis, 1)
    from_right = shift(x, axis, -1)
    half = x.shape[0] // 2
    far_lo = shift(from_left[:half], axis, 1)
    far_hi = shift(from_right[half:], axis, -1)
    buf = put(buf, x, base, buf_axis, me)
    buf = put(buf, from_left, base, buf_axis, (me + n - 1) % n)
    buf = put(buf, from_right, base, buf_axis, (me + 1) % n)
    far = (me + 2) % n
    buf = put(buf, far_lo, base, buf_axis, far)
    hi = list(base)
    inner = buf_axis + 1 if buf_axis == 0 else 0
    hi[inner] = hi[inner] + half
    buf = put(buf, far_hi, hi, buf_axis, far)
    return buf


def shards(packed_w, packed_t, row_energy, col_energy, block_order):
    nx = lax.axis_size("dx")
    ny = lax.axis_size("dy")
    ncore = lax.axis_size("dc")
    ngrp = lax.axis_size("grp")
    x = lax.axis_index("dx")
    y = lax.axis_index("dy")
    c = lax.axis_index("dc")
    z = lax.axis_index("grp")
    rank = (x * ny + y) * ncore + c
    local = packed_t.shape[1]
    ndev = nx * ny * ncore
    true_rows = jnp.arange(local, dtype=jnp.int32) * ndev + rank

    t_rows = lax.all_to_all(packed_t, "grp", split_axis=0, concat_axis=2, tiled=True)[0]
    order = lax.dynamic_index_in_dim(block_order, z, 0, keepdims=False)
    live = true_rows < order
    t_live = jnp.where(live[:, None], t_rows, jnp.zeros_like(t_rows))
    ncol = t_live.shape[1]

    half = local // 2
    col_a = ring4(t_live[:half], "dy", y, jnp.zeros((ny, half, ncol), t_live.dtype), 0, (0, 0, 0))
    row_b = ring4(t_live[half:], "dx", x, jnp.zeros((nx, half, ncol), t_live.dtype), 0, (0, 0, 0))
    t_abs = jnp.zeros((nx, ny, local, ncol), t_live.dtype)
    t_abs = ring4(col_a, "dx", x, t_abs, 0, (0, 0, 0, 0))
    t_abs = ring4(row_b, "dy", y, t_abs, 1, (0, 0, half, 0))

    w_in, _ = lax.optimization_barrier((packed_w, col_a))
    span = packed_w.shape[2] // ny
    cols = span // ncore
    w_all = jnp.zeros((ncore * local, nx * ny * cols), packed_w.dtype)
    for sz in range(ngrp):
        for sc in range(ncore):
            zt = (z + sz) % ngrp
            ct = (c + sc) % ncore
            piece = jnp.concatenate(
                [lax.dynamic_slice(w_in, (zt, 0, j * span + ct * cols), (1, local, cols))[0]
                 for j in range(ny)], axis=1)
            if sz or sc:
                n = ngrp * ncore
                perm = []
                for i in range(n):
                    gi, ci = divmod(i, ncore)
                    perm.append((i, ((gi + sz) % ngrp) * ncore + (ci + sc) % ncore))
                piece = lax.ppermute(piece, ("grp", "dc"), perm)
            where = ((z - sz) % ngrp) * (ny * cols)
            w_all = lax.dynamic_update_slice(w_all, piece, (sc * local, where))

    t_flat = t_abs.reshape(-1, ncol)
    partial = jnp.dot(w_all, t_flat, preferred_element_type=jnp.float32)
    mine = partial[:local]
    other = partial[local:]
    cycle = mine + shift(other, "dc", 1)
    new_block = apply_update(t_rows, cycle, live, row_energy[0], col_energy[0])
    return lax.all_to_all(new_block[None], "grp", split_axis=2, concat_axis=0, tiled=True)


def solution(mesh):
    ngrp, ndev = mesh.devices.shape
    ncore = 2
    nx = 4
    ny = ndev // (ncore * nx)
    split = Mesh(mesh.devices.reshape(ngrp, nx, ny, ncore), ("grp", "dx", "dy", "dc"))
    rows = ("dx", "dy", "dc")
    in_specs = (P(None, rows, "grp"), P(None, rows, "grp"), P("grp", rows), P("grp", None), P())
    out_specs = P(None, rows, "grp")
    body = jax.shard_map(shards, mesh=split, in_specs=in_specs, out_specs=out_specs, check_vma=False)
    target = NamedSharding(mesh, P(None, "dev", "grp"))

    def run(*args):
        return lax.with_sharding_constraint(body(*args), target)

    return run
```

```python
import jax
import jax.numpy as jnp
from jax import lax
from jax.sharding import Mesh, NamedSharding, PartitionSpec as P


def apply_update(t_rows, cycle, live, row_gap, col_gap):
    denom = row_gap[:, None] + col_gap[None, :]
    update = jnp.where(live[:, None], cycle / denom, jnp.zeros_like(cycle))
    return t_rows.astype(jnp.float32) + update


def shift(x, axis, step):
    n = lax.axis_size(axis)
    return lax.ppermute(x, axis, [(i, (i + step) % n) for i in range(n)])


def put(buf, piece, base, axis, index):
    start = list(base)
    start[axis] = index
    return lax.dynamic_update_slice(buf, jnp.expand_dims(piece, axis), start)


def ring4(x, axis, pos, buf, buf_axis, base):
    from_left = shift(x, axis, 1)
    from_right = shift(x, axis, -1)
    half = x.shape[0] // 2
    far_lo = shift(from_left[:half], axis, 1)
    far_hi = shift(from_right[half:], axis, -1)
    buf = put(buf, x, base, buf_axis, pos(0))
    buf = put(buf, from_left, base, buf_axis, pos(-1))
    buf = put(buf, from_right, base, buf_axis, pos(1))
    buf = put(buf, far_lo, base, buf_axis, pos(2))
    hi = list(base)
    inner = buf_axis + 1 if buf_axis == 0 else 0
    hi[inner] = hi[inner] + half
    buf = put(buf, far_hi, hi, buf_axis, pos(2))
    return buf


def shards(packed_w, packed_t, row_energy, col_energy, block_order):
    nx = lax.axis_size("dx")
    ny = lax.axis_size("dy")
    ncore = lax.axis_size("dc")
    ngrp = lax.axis_size("grp")
    x = lax.axis_index("dx")
    y = lax.axis_index("dy")
    c = lax.axis_index("dc")
    z = lax.axis_index("grp")
    rank = (x * ny + y) * ncore + c
    local = packed_t.shape[1]
    ndev = nx * ny * ncore
    true_rows = jnp.arange(local, dtype=jnp.int32) * ndev + rank

    t_rows = lax.all_to_all(packed_t, "grp", split_axis=0, concat_axis=2, tiled=True)[0]
    order = lax.dynamic_index_in_dim(block_order, z, 0, keepdims=False)
    live = true_rows < order
    t_live = jnp.where(live[:, None], t_rows, jnp.zeros_like(t_rows))
    ncol = t_live.shape[1]

    half = local // 2
    by_y = lambda o: (y + o) % ny
    by_x = lambda o: (z - x - o) % nx
    col_a = ring4(t_live[:half], "dy", by_y, jnp.zeros((ny, half, ncol), t_live.dtype), 0, (0, 0, 0))
    row_b = ring4(t_live[half:], "dx", by_x, jnp.zeros((nx, half, ncol), t_live.dtype), 0, (0, 0, 0))
    t_abs = jnp.zeros((nx, ny, local, ncol), t_live.dtype)
    t_abs = ring4(col_a, "dx", by_x, t_abs, 0, (0, 0, 0, 0))
    t_abs = ring4(row_b, "dy", by_y, t_abs, 1, (0, 0, half, 0))

    w_in, _ = lax.optimization_barrier((packed_w, col_a))
    span = packed_w.shape[2] // ny
    cols = span // ncore
    rows_of = []
    for sc in range(ncore):
        chunks = []
        for sz in range(ngrp):
            zt = (z + sz) % ngrp
            ct = (c + sc) % ncore
            piece = jnp.concatenate(
                [lax.dynamic_slice(w_in, (zt, 0, j * span + ct * cols), (1, local, cols))[0]
                 for j in range(ny)], axis=1)
            if sz or sc:
                n = ngrp * ncore
                perm = []
                for i in range(n):
                    gi, ci = divmod(i, ncore)
                    perm.append((i, ((gi + sz) % ngrp) * ncore + (ci + sc) % ncore))
                piece = lax.ppermute(piece, ("grp", "dc"), perm)
            chunks.append(piece)
        rows_of.append(jnp.concatenate(chunks, axis=1))
    w_all = jnp.concatenate(rows_of, axis=0)

    t_flat = t_abs.reshape(-1, ncol)
    partial = jnp.dot(w_all, t_flat, preferred_element_type=jnp.float32)
    mine = partial[:local]
    other = partial[local:]
    cycle = mine + shift(other, "dc", 1)
    new_block = apply_update(t_rows, cycle, live, row_energy[0], col_energy[0])
    return lax.all_to_all(new_block[None], "grp", split_axis=2, concat_axis=0, tiled=True)


def solution(mesh):
    ngrp, ndev = mesh.devices.shape
    ncore = 2
    nx = 4
    ny = ndev // (ncore * nx)
    split = Mesh(mesh.devices.reshape(ngrp, nx, ny, ncore), ("grp", "dx", "dy", "dc"))
    rows = ("dx", "dy", "dc")
    in_specs = (P(None, rows, "grp"), P(None, rows, "grp"), P("grp", rows), P("grp", None), P())
    out_specs = P(None, rows, "grp")
    body = jax.shard_map(shards, mesh=split, in_specs=in_specs, out_specs=out_specs, check_vma=False)
    target = NamedSharding(mesh, P(None, "dev", "grp"))

    def run(*args):
        return lax.with_sharding_constraint(body(*args), target)

    return run
```

```python
import jax
import jax.numpy as jnp
from jax import lax
from jax.sharding import Mesh, NamedSharding, PartitionSpec as P


def apply_update(t_rows, cycle, live, row_gap, col_gap):
    denom = row_gap[:, None] + col_gap[None, :]
    update = jnp.where(live[:, None], cycle / denom, jnp.zeros_like(cycle))
    return t_rows.astype(jnp.float32) + update


def shift(x, axis, step):
    n = lax.axis_size(axis)
    return lax.ppermute(x, axis, [(i, (i + step) % n) for i in range(n)])


def put(buf, piece, base, axis, index):
    start = list(base)
    start[axis] = index
    return lax.dynamic_update_slice(buf, jnp.expand_dims(piece, axis), start)


def hop(piece, ngrp, ncore, sz, sc):
    perm = []
    for i in range(ngrp * ncore):
        gi, ci = divmod(i, ncore)
        perm.append((i, ((gi + sz) % ngrp) * ncore + (ci + sc) % ncore))
    return lax.ppermute(piece, ("grp", "dc"), perm)


def ring4(x, axis, pos, buf, buf_axis, base):
    from_left = shift(x, axis, 1)
    from_right = shift(x, axis, -1)
    half = x.shape[0] // 2
    far_lo = shift(from_left[:half], axis, 1)
    far_hi = shift(from_right[half:], axis, -1)
    buf = put(buf, x, base, buf_axis, pos(0))
    buf = put(buf, from_left, base, buf_axis, pos(-1))
    buf = put(buf, from_right, base, buf_axis, pos(1))
    buf = put(buf, far_lo, base, buf_axis, pos(2))
    hi = list(base)
    inner = buf_axis + 1 if buf_axis == 0 else 0
    hi[inner] = hi[inner] + half
    buf = put(buf, far_hi, hi, buf_axis, pos(2))
    return buf


def shards(packed_w, packed_t, row_energy, col_energy, block_order):
    nx = lax.axis_size("dx")
    ny = lax.axis_size("dy")
    ncore = lax.axis_size("dc")
    ngrp = lax.axis_size("grp")
    x = lax.axis_index("dx")
    y = lax.axis_index("dy")
    c = lax.axis_index("dc")
    z = lax.axis_index("grp")
    rank = (x * ny + y) * ncore + c
    local = packed_t.shape[1]
    ndev = nx * ny * ncore
    true_rows = jnp.arange(local, dtype=jnp.int32) * ndev + rank

    t_rows = lax.all_to_all(packed_t, "grp", split_axis=0, concat_axis=2, tiled=True)[0]
    order = lax.dynamic_index_in_dim(block_order, z, 0, keepdims=False)
    live = true_rows < order
    t_live = jnp.where(live[:, None], t_rows, jnp.zeros_like(t_rows))
    ncol = t_live.shape[1]

    half = local // 2
    by_y = lambda o: (y + o) % ny
    by_x = lambda o: (z - x - o) % nx
    col_a = ring4(t_live[:half], "dy", by_y, jnp.zeros((ny, half, ncol), t_live.dtype), 0, (0, 0, 0))
    row_b = ring4(t_live[half:], "dx", by_x, jnp.zeros((nx, half, ncol), t_live.dtype), 0, (0, 0, 0))
    t_abs = jnp.zeros((nx, ny, local, ncol), t_live.dtype)
    t_abs = ring4(col_a, "dx", by_x, t_abs, 0, (0, 0, 0, 0))
    t_abs = ring4(row_b, "dy", by_y, t_abs, 1, (0, 0, half, 0))

    w_in, _ = lax.optimization_barrier((packed_w, t_live))
    span = packed_w.shape[2] // ny
    cols = span // ncore
    rows_of = []
    for sc in range(ncore):
        chunks = []
        for sz in range(ngrp):
            zt = (z + sz) % ngrp
            ct = (c + sc) % ncore
            piece = jnp.concatenate(
                [lax.dynamic_slice(w_in, (zt, 0, j * span + ct * cols), (1, local, cols))[0]
                 for j in range(ny)], axis=1)
            if sz * 2 == ngrp:
                way = 1 if sc == 0 else -1
                piece = hop(piece, ngrp, ncore, way, sc)
                piece = hop(piece, ngrp, ncore, way, 0)
            elif sz or sc:
                piece = hop(piece, ngrp, ncore, sz, sc)
            chunks.append(piece)
        rows_of.append(jnp.concatenate(chunks, axis=1))
    w_all = jnp.concatenate(rows_of, axis=0)

    t_flat = t_abs.reshape(-1, ncol)
    partial = jnp.dot(w_all, t_flat, preferred_element_type=jnp.float32)
    mine = partial[:local]
    other = partial[local:]
    cycle = mine + shift(other, "dc", 1)
    new_block = apply_update(t_rows, cycle, live, row_energy[0], col_energy[0])
    return lax.all_to_all(new_block[None], "grp", split_axis=2, concat_axis=0, tiled=True)


def solution(mesh):
    ngrp, ndev = mesh.devices.shape
    ncore = 2
    nx = 4
    ny = ndev // (ncore * nx)
    split = Mesh(mesh.devices.reshape(ngrp, nx, ny, ncore), ("grp", "dx", "dy", "dc"))
    rows = ("dx", "dy", "dc")
    in_specs = (P(None, rows, "grp"), P(None, rows, "grp"), P("grp", rows), P("grp", None), P())
    out_specs = P(None, rows, "grp")
    body = jax.shard_map(shards, mesh=split, in_specs=in_specs, out_specs=out_specs, check_vma=False)
    target = NamedSharding(mesh, P(None, "dev", "grp"))

    def run(*args):
        return lax.with_sharding_constraint(body(*args), target)

    return run
```

```python
import jax
import jax.numpy as jnp
from jax import lax
from jax.sharding import Mesh, NamedSharding, PartitionSpec as P


def apply_update(t_rows, cycle, live, row_gap, col_gap):
    denom = row_gap[:, None] + col_gap[None, :]
    update = jnp.where(live[:, None], cycle / denom, jnp.zeros_like(cycle))
    return t_rows.astype(jnp.float32) + update


def shift(x, axis, step):
    n = lax.axis_size(axis)
    return lax.ppermute(x, axis, [(i, (i + step) % n) for i in range(n)])


def put(buf, piece, base, axis, index):
    start = list(base)
    start[axis] = index
    return lax.dynamic_update_slice(buf, jnp.expand_dims(piece, axis), start)


def hop(piece, ngrp, ncore, sz, sc):
    perm = []
    for i in range(ngrp * ncore):
        gi, ci = divmod(i, ncore)
        perm.append((i, ((gi + sz) % ngrp) * ncore + (ci + sc) % ncore))
    return lax.ppermute(piece, ("grp", "dc"), perm)


def ring4(x, axis, pos, buf, buf_axis, base, keep_far=False):
    from_left = shift(x, axis, 1)
    from_right = shift(x, axis, -1)
    half = x.shape[0] // 2
    far_lo = shift(from_left[:half], axis, 1)
    far_hi = shift(from_right[half:], axis, -1)
    buf = put(buf, x, base, buf_axis, pos(0))
    buf = put(buf, from_left, base, buf_axis, pos(-1))
    buf = put(buf, from_right, base, buf_axis, pos(1))
    if keep_far:
        return buf, jnp.concatenate([far_lo, far_hi], axis=0)
    buf = put(buf, far_lo, base, buf_axis, pos(2))
    hi = list(base)
    inner = buf_axis + 1 if buf_axis == 0 else 0
    hi[inner] = hi[inner] + half
    buf = put(buf, far_hi, hi, buf_axis, pos(2))
    return buf


def shards(packed_w, packed_t, row_energy, col_energy, block_order):
    nx = lax.axis_size("dx")
    ny = lax.axis_size("dy")
    ncore = lax.axis_size("dc")
    ngrp = lax.axis_size("grp")
    x = lax.axis_index("dx")
    y = lax.axis_index("dy")
    c = lax.axis_index("dc")
    z = lax.axis_index("grp")
    rank = (x * ny + y) * ncore + c
    local = packed_t.shape[1]
    ndev = nx * ny * ncore
    true_rows = jnp.arange(local, dtype=jnp.int32) * ndev + rank

    t_rows = lax.all_to_all(packed_t, "grp", split_axis=0, concat_axis=2, tiled=True)[0]
    order = lax.dynamic_index_in_dim(block_order, z, 0, keepdims=False)
    live = true_rows < order
    t_live = jnp.where(live[:, None], t_rows, jnp.zeros_like(t_rows))
    ncol = t_live.shape[1]

    half = local // 2
    by_y = lambda o: (y + o) % ny
    by_x = lambda o: (z - x - o) % nx
    col_a = ring4(t_live[:half], "dy", by_y, jnp.zeros((ny, half, ncol), t_live.dtype), 0, (0, 0, 0))
    row_b = ring4(t_live[half:], "dx", by_x, jnp.zeros((nx, half, ncol), t_live.dtype), 0, (0, 0, 0))
    t_abs = jnp.zeros((nx, ny, local, ncol), t_live.dtype)
    t_abs, far_a = ring4(col_a, "dx", by_x, t_abs, 0, (0, 0, 0, 0), keep_far=True)
    t_abs, far_b = ring4(row_b, "dy", by_y, t_abs, 1, (0, 0, half, 0), keep_far=True)

    w_in, _ = lax.optimization_barrier((packed_w, t_live))
    span = packed_w.shape[2] // ny
    cols = span // ncore
    rows_of = []
    for sc in range(ncore):
        chunks = []
        for sz in range(ngrp):
            zt = (z + sz) % ngrp
            ct = (c + sc) % ncore
            piece = jnp.concatenate(
                [lax.dynamic_slice(w_in, (zt, 0, j * span + ct * cols), (1, local, cols))[0]
                 for j in range(ny)], axis=1)
            if sz * 2 == ngrp:
                way = 1 if sc == 0 else -1
                piece = hop(piece, ngrp, ncore, way, sc)
                piece = hop(piece, ngrp, ncore, way, 0)
            elif sz or sc:
                piece = hop(piece, ngrp, ncore, sz, sc)
            chunks.append(piece)
        rows_of.append(jnp.concatenate(chunks, axis=1))
    w_all = jnp.concatenate(rows_of, axis=0)

    w_all = lax.optimization_barrier(w_all)

    t_flat = t_abs.reshape(-1, ncol)
    partial = jnp.dot(w_all, t_flat, preferred_element_type=jnp.float32)
    chunk = ny * local
    ka = by_x(2)
    w_fa = jnp.concatenate(
        [lax.dynamic_slice_in_dim(w_all, ka * chunk + j * local, half, 1) for j in range(ny)], axis=1)
    yb = by_y(2)
    w_fb = jnp.concatenate(
        [lax.dynamic_slice_in_dim(w_all, k * chunk + yb * local + half, half, 1) for k in range(nx)], axis=1)
    partial = partial + jnp.dot(w_fa, far_a.reshape(-1, ncol), preferred_element_type=jnp.float32)
    partial = partial + jnp.dot(w_fb, far_b.reshape(-1, ncol), preferred_element_type=jnp.float32)
    mine = partial[:local]
    other = partial[local:]
    cycle = mine + shift(other, "dc", 1)
    new_block = apply_update(t_rows, cycle, live, row_energy[0], col_energy[0])
    return lax.all_to_all(new_block[None], "grp", split_axis=2, concat_axis=0, tiled=True)


def solution(mesh):
    ngrp, ndev = mesh.devices.shape
    ncore = 2
    nx = 4
    ny = ndev // (ncore * nx)
    split = Mesh(mesh.devices.reshape(ngrp, nx, ny, ncore), ("grp", "dx", "dy", "dc"))
    rows = ("dx", "dy", "dc")
    in_specs = (P(None, rows, "grp"), P(None, rows, "grp"), P("grp", rows), P("grp", None), P())
    out_specs = P(None, rows, "grp")
    body = jax.shard_map(shards, mesh=split, in_specs=in_specs, out_specs=out_specs, check_vma=False)
    target = NamedSharding(mesh, P(None, "dev", "grp"))

    def run(*args):
        return lax.with_sharding_constraint(body(*args), target)

    return run
```

```python
import jax
import jax.numpy as jnp
from jax import lax
from jax.sharding import Mesh, NamedSharding, PartitionSpec as P


def apply_update(t_rows, cycle, live, row_gap, col_gap):
    denom = row_gap[:, None] + col_gap[None, :]
    update = jnp.where(live[:, None], cycle / denom, jnp.zeros_like(cycle))
    return t_rows.astype(jnp.float32) + update


def shift(x, axis, step):
    n = lax.axis_size(axis)
    return lax.ppermute(x, axis, [(i, (i + step) % n) for i in range(n)])


def put(buf, piece, base, axis, index):
    start = list(base)
    start[axis] = index
    return lax.dynamic_update_slice(buf, jnp.expand_dims(piece, axis), start)


def hop(piece, ngrp, ncore, sz, sc):
    perm = []
    for i in range(ngrp * ncore):
        gi, ci = divmod(i, ncore)
        perm.append((i, ((gi + sz) % ngrp) * ncore + (ci + sc) % ncore))
    return lax.ppermute(piece, ("grp", "dc"), perm)


def ring4(x, axis, pos, buf, buf_axis, base):
    from_left = shift(x, axis, 1)
    from_right = shift(x, axis, -1)
    half = x.shape[0] // 2
    far_lo = shift(from_left[:half], axis, 1)
    far_hi = shift(from_right[half:], axis, -1)
    buf = put(buf, x, base, buf_axis, pos(0))
    buf = put(buf, from_left, base, buf_axis, pos(-1))
    buf = put(buf, from_right, base, buf_axis, pos(1))
    buf = put(buf, far_lo, base, buf_axis, pos(2))
    hi = list(base)
    inner = buf_axis + 1 if buf_axis == 0 else 0
    hi[inner] = hi[inner] + half
    buf = put(buf, far_hi, hi, buf_axis, pos(2))
    return buf


def shards(packed_w, packed_t, row_energy, col_energy, block_order):
    nx = lax.axis_size("dx")
    ny = lax.axis_size("dy")
    ncore = lax.axis_size("dc")
    ngrp = lax.axis_size("grp")
    x = lax.axis_index("dx")
    y = lax.axis_index("dy")
    c = lax.axis_index("dc")
    z = lax.axis_index("grp")
    rank = (x * ny + y) * ncore + c
    local = packed_t.shape[1]
    ndev = nx * ny * ncore
    true_rows = jnp.arange(local, dtype=jnp.int32) * ndev + rank

    t_rows = lax.all_to_all(packed_t, "grp", split_axis=0, concat_axis=2, tiled=True)[0]
    order = lax.dynamic_index_in_dim(block_order, z, 0, keepdims=False)
    live = true_rows < order
    t_live = jnp.where(live[:, None], t_rows, jnp.zeros_like(t_rows))
    ncol = t_live.shape[1]

    half = local // 2
    by_y = lambda o: (y + o) % ny
    by_x = lambda o: (z - x - o) % nx
    col_a = ring4(t_live[:half], "dy", by_y, jnp.zeros((ny, half, ncol), t_live.dtype), 0, (0, 0, 0))
    row_b = ring4(t_live[half:], "dx", by_x, jnp.zeros((nx, half, ncol), t_live.dtype), 0, (0, 0, 0))
    t_abs = jnp.zeros((nx, ny, local, ncol), t_live.dtype)
    t_abs = ring4(col_a, "dx", by_x, t_abs, 0, (0, 0, 0, 0))
    t_abs = ring4(row_b, "dy", by_y, t_abs, 1, (0, 0, half, 0))

    w_in, _ = lax.optimization_barrier((packed_w, t_live))
    span = packed_w.shape[2] // ny
    cols = span // ncore
    rows_of = []
    for sc in range(ncore):
        chunks = []
        for sz in range(ngrp):
            zt = (z + sz) % ngrp
            ct = (c + sc) % ncore
            piece = jnp.concatenate(
                [lax.dynamic_slice(w_in, (zt, 0, j * span + ct * cols), (1, local, cols))[0]
                 for j in range(ny)], axis=1)
            if sz * 2 == ngrp:
                way = 1 if sc == 0 else -1
                piece = hop(piece, ngrp, ncore, way, sc)
                piece = hop(piece, ngrp, ncore, way, 0)
            elif sz or sc:
                piece = hop(piece, ngrp, ncore, sz, sc)
            chunks.append(piece)
        rows_of.append(jnp.concatenate(chunks, axis=1))
    w_all = lax.optimization_barrier(jnp.concatenate(rows_of, axis=0))

    t_flat = t_abs.reshape(-1, ncol)
    partial = jnp.dot(w_all, t_flat, preferred_element_type=jnp.float32)
    mine = partial[:local]
    other = partial[local:]
    cycle = mine + shift(other, "dc", 1)
    new_block = apply_update(t_rows, cycle, live, row_energy[0], col_energy[0])

    width = new_block.shape[1] // ngrp
    out = jnp.zeros((ngrp, local, width), new_block.dtype)
    for sz in range(ngrp):
        piece = lax.dynamic_slice_in_dim(new_block, ((z + sz) % ngrp) * width, width, 1)
        if sz * 2 == ngrp:
            lo = shift(shift(piece[:half], "grp", 1), "grp", 1)
            hi = shift(shift(piece[half:], "grp", -1), "grp", -1)
            piece = jnp.concatenate([lo, hi], axis=0)
        elif sz:
            piece = shift(piece, "grp", sz)
        out = lax.dynamic_update_slice(out, piece[None], ((z - sz) % ngrp, 0, 0))
    return out


def solution(mesh):
    ngrp, ndev = mesh.devices.shape
    ncore = 2
    nx = 4
    ny = ndev // (ncore * nx)
    split = Mesh(mesh.devices.reshape(ngrp, nx, ny, ncore), ("grp", "dx", "dy", "dc"))
    rows = ("dx", "dy", "dc")
    in_specs = (P(None, rows, "grp"), P(None, rows, "grp"), P("grp", rows), P("grp", None), P())
    out_specs = P(None, rows, "grp")
    body = jax.shard_map(shards, mesh=split, in_specs=in_specs, out_specs=out_specs, check_vma=False)
    target = NamedSharding(mesh, P(None, "dev", "grp"))

    def run(*args):
        return lax.with_sharding_constraint(body(*args), target)

    return run
```

```python
import jax
import jax.numpy as jnp
from jax import lax
from jax.sharding import Mesh, NamedSharding, PartitionSpec as P


def apply_update(t_rows, cycle, live, row_gap, col_gap):
    denom = row_gap[:, None] + col_gap[None, :]
    update = jnp.where(live[:, None], cycle / denom, jnp.zeros_like(cycle))
    return t_rows.astype(jnp.float32) + update


def shift(x, axis, step):
    n = lax.axis_size(axis)
    return lax.ppermute(x, axis, [(i, (i + step) % n) for i in range(n)])


def put(buf, piece, base, axis, index):
    start = list(base)
    start[axis] = index
    return lax.dynamic_update_slice(buf, jnp.expand_dims(piece, axis), start)


def hop(piece, ngrp, ncore, sz, sc):
    perm = []
    for i in range(ngrp * ncore):
        gi, ci = divmod(i, ncore)
        perm.append((i, ((gi + sz) % ngrp) * ncore + (ci + sc) % ncore))
    return lax.ppermute(piece, ("grp", "dc"), perm)


def ring4(x, axis, pos, buf, buf_axis, base, near=None):
    from_left = shift(x, axis, 1)
    from_right = shift(x, axis, -1)
    if near is not None:
        near.extend([from_left, from_right])
    half = x.shape[0] // 2
    far_lo = shift(from_left[:half], axis, 1)
    far_hi = shift(from_right[half:], axis, -1)
    buf = put(buf, x, base, buf_axis, pos(0))
    buf = put(buf, from_left, base, buf_axis, pos(-1))
    buf = put(buf, from_right, base, buf_axis, pos(1))
    buf = put(buf, far_lo, base, buf_axis, pos(2))
    hi = list(base)
    inner = buf_axis + 1 if buf_axis == 0 else 0
    hi[inner] = hi[inner] + half
    buf = put(buf, far_hi, hi, buf_axis, pos(2))
    return buf


def shards(packed_w, packed_t, row_energy, col_energy, block_order):
    nx = lax.axis_size("dx")
    ny = lax.axis_size("dy")
    ncore = lax.axis_size("dc")
    ngrp = lax.axis_size("grp")
    x = lax.axis_index("dx")
    y = lax.axis_index("dy")
    c = lax.axis_index("dc")
    z = lax.axis_index("grp")
    rank = (x * ny + y) * ncore + c
    local = packed_t.shape[1]
    ndev = nx * ny * ncore
    true_rows = jnp.arange(local, dtype=jnp.int32) * ndev + rank

    t_rows = lax.all_to_all(packed_t, "grp", split_axis=0, concat_axis=2, tiled=True)[0]
    order = lax.dynamic_index_in_dim(block_order, z, 0, keepdims=False)
    live = true_rows < order
    t_live = jnp.where(live[:, None], t_rows, jnp.zeros_like(t_rows))
    ncol = t_live.shape[1]

    half = local // 2
    by_y = lambda o: (y + o) % ny
    by_x = lambda o: (z - x - o) % nx
    col_a = ring4(t_live[:half], "dy", by_y, jnp.zeros((ny, half, ncol), t_live.dtype), 0, (0, 0, 0))
    row_b = ring4(t_live[half:], "dx", by_x, jnp.zeros((nx, half, ncol), t_live.dtype), 0, (0, 0, 0))
    t_abs = jnp.zeros((nx, ny, local, ncol), t_live.dtype)
    near = []
    t_abs = ring4(col_a, "dx", by_x, t_abs, 0, (0, 0, 0, 0), near)
    t_abs = ring4(row_b, "dy", by_y, t_abs, 1, (0, 0, half, 0), near)

    w_in, _ = lax.optimization_barrier((packed_w, t_live))
    span = packed_w.shape[2] // ny
    cols = span // ncore
    rows_of = []
    for sc in range(ncore):
        chunks = []
        for sz in range(ngrp):
            zt = (z + sz) % ngrp
            ct = (c + sc) % ncore
            piece = jnp.concatenate(
                [lax.dynamic_slice(w_in, (zt, 0, j * span + ct * cols), (1, local, cols))[0]
                 for j in range(ny)], axis=1)
            if sz * 2 == ngrp:
                way = 1 if sc == 0 else -1
                piece = hop(piece, ngrp, ncore, way, sc)
                piece = hop(piece, ngrp, ncore, way, 0)
            elif sz or sc:
                piece = hop(piece, ngrp, ncore, sz, sc)
            chunks.append(piece)
        rows_of.append(jnp.concatenate(chunks, axis=1))
    rows_of, _ = lax.optimization_barrier((rows_of, near))
    w_all = lax.optimization_barrier(jnp.concatenate(rows_of, axis=0))

    t_flat = t_abs.reshape(-1, ncol)
    partial = jnp.dot(w_all, t_flat, preferred_element_type=jnp.float32)
    mine = partial[:local]
    other = partial[local:]
    cycle = mine + shift(other, "dc", 1)
    new_block = apply_update(t_rows, cycle, live, row_energy[0], col_energy[0])

    width = new_block.shape[1] // ngrp
    out = jnp.zeros((ngrp, local, width), new_block.dtype)
    for sz in range(ngrp):
        piece = lax.dynamic_slice_in_dim(new_block, ((z + sz) % ngrp) * width, width, 1)
        if sz * 2 == ngrp:
            lo = shift(shift(piece[:half], "grp", 1), "grp", 1)
            hi = shift(shift(piece[half:], "grp", -1), "grp", -1)
            piece = jnp.concatenate([lo, hi], axis=0)
        elif sz:
            piece = shift(piece, "grp", sz)
        out = lax.dynamic_update_slice(out, piece[None], ((z - sz) % ngrp, 0, 0))
    return out


def solution(mesh):
    ngrp, ndev = mesh.devices.shape
    ncore = 2
    nx = 4
    ny = ndev // (ncore * nx)
    split = Mesh(mesh.devices.reshape(ngrp, nx, ny, ncore), ("grp", "dx", "dy", "dc"))
    rows = ("dx", "dy", "dc")
    in_specs = (P(None, rows, "grp"), P(None, rows, "grp"), P("grp", rows), P("grp", None), P())
    out_specs = P(None, rows, "grp")
    body = jax.shard_map(shards, mesh=split, in_specs=in_specs, out_specs=out_specs, check_vma=False)
    target = NamedSharding(mesh, P(None, "dev", "grp"))

    def run(*args):
        return lax.with_sharding_constraint(body(*args), target)

    return run
```

```python
import jax
import jax.numpy as jnp
from jax import lax
from jax.sharding import Mesh, NamedSharding, PartitionSpec as P


def apply_update(t_rows, cycle, live, row_gap, col_gap):
    denom = row_gap[:, None] + col_gap[None, :]
    update = jnp.where(live[:, None], cycle / denom, jnp.zeros_like(cycle))
    return t_rows.astype(jnp.float32) + update


def shift(x, axis, step):
    n = lax.axis_size(axis)
    return lax.ppermute(x, axis, [(i, (i + step) % n) for i in range(n)])


def put(buf, piece, base, axis, index):
    start = list(base)
    start[axis] = index
    return lax.dynamic_update_slice(buf, jnp.expand_dims(piece, axis), start)


def hop(piece, ngrp, ncore, sz, sc):
    perm = []
    for i in range(ngrp * ncore):
        gi, ci = divmod(i, ncore)
        perm.append((i, ((gi + sz) % ngrp) * ncore + (ci + sc) % ncore))
    return lax.ppermute(piece, ("grp", "dc"), perm)


def ring4(x, axis, pos, buf, buf_axis, base, near=None):
    from_left = shift(x, axis, 1)
    from_right = shift(x, axis, -1)
    if near is not None:
        near.extend([from_left, from_right])
    half = x.shape[0] // 2
    far_lo = shift(from_left[:half], axis, 1)
    far_hi = shift(from_right[half:], axis, -1)
    buf = put(buf, x, base, buf_axis, pos(0))
    buf = put(buf, from_left, base, buf_axis, pos(-1))
    buf = put(buf, from_right, base, buf_axis, pos(1))
    buf = put(buf, far_lo, base, buf_axis, pos(2))
    hi = list(base)
    inner = buf_axis + 1 if buf_axis == 0 else 0
    hi[inner] = hi[inner] + half
    buf = put(buf, far_hi, hi, buf_axis, pos(2))
    return buf


def shards(packed_w, packed_t, row_energy, col_energy, block_order):
    nx = lax.axis_size("dx")
    ny = lax.axis_size("dy")
    ncore = lax.axis_size("dc")
    ngrp = lax.axis_size("grp")
    x = lax.axis_index("dx")
    y = lax.axis_index("dy")
    c = lax.axis_index("dc")
    z = lax.axis_index("grp")
    rank = (x * ny + y) * ncore + c
    local = packed_t.shape[1]
    ndev = nx * ny * ncore
    true_rows = jnp.arange(local, dtype=jnp.int32) * ndev + rank

    t_rows = lax.all_to_all(packed_t, "grp", split_axis=0, concat_axis=2, tiled=True)[0]
    order = lax.dynamic_index_in_dim(block_order, z, 0, keepdims=False)
    live = true_rows < order
    t_live = jnp.where(live[:, None], t_rows, jnp.zeros_like(t_rows))
    ncol = t_live.shape[1]

    half = local // 2
    by_y = lambda o: (y + o) % ny
    by_x = lambda o: (z - x - o) % nx
    col_a = ring4(t_live[:half], "dy", by_y, jnp.zeros((ny, half, ncol), t_live.dtype), 0, (0, 0, 0))
    row_b = ring4(t_live[half:], "dx", by_x, jnp.zeros((nx, half, ncol), t_live.dtype), 0, (0, 0, 0))
    t_abs = jnp.zeros((nx, ny, local, ncol), t_live.dtype)
    near = []
    t_abs = ring4(col_a, "dx", by_x, t_abs, 0, (0, 0, 0, 0), near)
    t_abs = ring4(row_b, "dy", by_y, t_abs, 1, (0, 0, half, 0), near)

    w_in, _ = lax.optimization_barrier((packed_w, t_live))
    span = packed_w.shape[2] // ny
    cols = span // ncore
    rows_of = []
    for sc in range(ncore):
        chunks = []
        for sz in range(ngrp):
            zt = (z + sz) % ngrp
            ct = (c + sc) % ncore
            piece = jnp.concatenate(
                [lax.dynamic_slice(w_in, (zt, 0, j * span + ct * cols), (1, local, cols))[0]
                 for j in range(ny)], axis=1)
            if sz * 2 == ngrp:
                way = 1 if sc == 0 else -1
                piece = hop(piece, ngrp, ncore, way, sc)
                piece = hop(piece, ngrp, ncore, way, 0)
            elif sz or sc:
                piece = hop(piece, ngrp, ncore, sz, sc)
            chunks.append(piece)
        rows_of.append(jnp.concatenate(chunks, axis=1))
    rows_of, _ = lax.optimization_barrier((rows_of, near))
    w_all = lax.optimization_barrier(jnp.concatenate(rows_of, axis=0))

    t_flat = t_abs.reshape(-1, ncol)
    row_gap = row_energy[0]
    col_gap = col_energy[0]

    width = ncol // ngrp
    out = jnp.zeros((ngrp, local, width), jnp.float32)
    for sz in (2, 1, 3, 0):
        at = ((z + sz) % ngrp) * width
        partial = jnp.dot(w_all, lax.dynamic_slice_in_dim(t_flat, at, width, 1),
                          preferred_element_type=jnp.float32)
        cycle = partial[:local] + shift(partial[local:], "dc", 1)
        piece = apply_update(lax.dynamic_slice_in_dim(t_rows, at, width, 1), cycle, live,
                             row_gap, lax.dynamic_slice_in_dim(col_gap, at, width, 0))
        if sz * 2 == ngrp:
            lo = shift(shift(piece[:half], "grp", 1), "grp", 1)
            hi = shift(shift(piece[half:], "grp", -1), "grp", -1)
            piece = jnp.concatenate([lo, hi], axis=0)
        elif sz:
            piece = shift(piece, "grp", sz)
        out = lax.dynamic_update_slice(out, piece[None], ((z - sz) % ngrp, 0, 0))
    return out


def solution(mesh):
    ngrp, ndev = mesh.devices.shape
    ncore = 2
    nx = 4
    ny = ndev // (ncore * nx)
    split = Mesh(mesh.devices.reshape(ngrp, nx, ny, ncore), ("grp", "dx", "dy", "dc"))
    rows = ("dx", "dy", "dc")
    in_specs = (P(None, rows, "grp"), P(None, rows, "grp"), P("grp", rows), P("grp", None), P())
    out_specs = P(None, rows, "grp")
    body = jax.shard_map(shards, mesh=split, in_specs=in_specs, out_specs=out_specs, check_vma=False)
    target = NamedSharding(mesh, P(None, "dev", "grp"))

    def run(*args):
        return lax.with_sharding_constraint(body(*args), target)

    return run
```

```python
import jax
import jax.numpy as jnp
from jax import lax
from jax.sharding import Mesh, NamedSharding, PartitionSpec as P


def apply_update(t_rows, cycle, live, row_gap, col_gap):
    denom = row_gap[:, None] + col_gap[None, :]
    update = jnp.where(live[:, None], cycle / denom, jnp.zeros_like(cycle))
    return t_rows.astype(jnp.float32) + update


def shift(x, axis, step):
    n = lax.axis_size(axis)
    return lax.ppermute(x, axis, [(i, (i + step) % n) for i in range(n)])


def put(buf, piece, base, axis, index):
    start = list(base)
    start[axis] = index
    return lax.dynamic_update_slice(buf, jnp.expand_dims(piece, axis), start)


def hop(piece, ngrp, ncore, sz, sc):
    perm = []
    for i in range(ngrp * ncore):
        gi, ci = divmod(i, ncore)
        perm.append((i, ((gi + sz) % ngrp) * ncore + (ci + sc) % ncore))
    return lax.ppermute(piece, ("grp", "dc"), perm)


def ring4(x, axis, pos, buf, buf_axis, base, near=None):
    from_left = shift(x, axis, 1)
    from_right = shift(x, axis, -1)
    if near is not None:
        near.extend([from_left, from_right])
    half = x.shape[0] // 2
    far_lo = shift(from_left[:half], axis, 1)
    far_hi = shift(from_right[half:], axis, -1)
    buf = put(buf, x, base, buf_axis, pos(0))
    buf = put(buf, from_left, base, buf_axis, pos(-1))
    buf = put(buf, from_right, base, buf_axis, pos(1))
    buf = put(buf, far_lo, base, buf_axis, pos(2))
    hi = list(base)
    inner = buf_axis + 1 if buf_axis == 0 else 0
    hi[inner] = hi[inner] + half
    buf = put(buf, far_hi, hi, buf_axis, pos(2))
    return buf


def shards(packed_w, packed_t, row_energy, col_energy, block_order):
    nx = lax.axis_size("dx")
    ny = lax.axis_size("dy")
    ncore = lax.axis_size("dc")
    ngrp = lax.axis_size("grp")
    x = lax.axis_index("dx")
    y = lax.axis_index("dy")
    c = lax.axis_index("dc")
    z = lax.axis_index("grp")
    rank = (x * ny + y) * ncore + c
    local = packed_t.shape[1]
    ndev = nx * ny * ncore
    true_rows = jnp.arange(local, dtype=jnp.int32) * ndev + rank

    t_rows = lax.all_to_all(packed_t, "grp", split_axis=0, concat_axis=2, tiled=True)[0]
    order = lax.dynamic_index_in_dim(block_order, z, 0, keepdims=False)
    live = true_rows < order
    t_live = jnp.where(live[:, None], t_rows, jnp.zeros_like(t_rows))
    ncol = t_live.shape[1]

    half = local // 2
    by_y = lambda o: (y + o) % ny
    by_x = lambda o: (z - x - o) % nx
    col_a = ring4(t_live[:half], "dy", by_y, jnp.zeros((ny, half, ncol), t_live.dtype), 0, (0, 0, 0))
    row_b = ring4(t_live[half:], "dx", by_x, jnp.zeros((nx, half, ncol), t_live.dtype), 0, (0, 0, 0))
    t_abs = jnp.zeros((nx, ny, local, ncol), t_live.dtype)
    near = []
    t_abs = ring4(col_a, "dx", by_x, t_abs, 0, (0, 0, 0, 0), near)
    t_abs = ring4(row_b, "dy", by_y, t_abs, 1, (0, 0, half, 0), near)

    w_in, _ = lax.optimization_barrier((packed_w, t_live))
    span = packed_w.shape[2] // ny
    cols = span // ncore
    rows_of = []
    for sc in range(ncore):
        chunks = []
        for sz in range(ngrp):
            zt = (z + sz) % ngrp
            ct = (c + sc) % ncore
            piece = jnp.concatenate(
                [lax.dynamic_slice(w_in, (zt, 0, j * span + ct * cols), (1, local, cols))[0]
                 for j in range(ny)], axis=1)
            if sz * 2 == ngrp:
                way = 1 if sc == 0 else -1
                piece = hop(piece, ngrp, ncore, way, sc)
                piece = hop(piece, ngrp, ncore, way, 0)
            elif sz or sc:
                piece = hop(piece, ngrp, ncore, sz, sc)
            chunks.append(piece)
        rows_of.append(jnp.concatenate(chunks, axis=1))
    rows_of, _ = lax.optimization_barrier((rows_of, near))
    w_all = lax.optimization_barrier(jnp.concatenate(rows_of, axis=0))

    t_flat = t_abs.reshape(-1, ncol)
    row_gap = row_energy[0]
    col_gap = col_energy[0]

    width = ncol // ngrp
    out = jnp.zeros((ngrp, local, width), jnp.float32)
    for sz in (2, 1, 3, 0):
        at = ((z + sz) % ngrp) * width
        partial = jnp.dot(w_all, lax.dynamic_slice_in_dim(t_flat, at, width, 1),
                          preferred_element_type=jnp.float32)
        cycle = partial[:local] + shift(partial[local:], "dc", 1)
        piece = apply_update(lax.dynamic_slice_in_dim(t_rows, at, width, 1), cycle, live,
                             row_gap, lax.dynamic_slice_in_dim(col_gap, at, width, 0))
        if sz:
            piece = shift(piece, "grp", sz)
        out = lax.dynamic_update_slice(out, piece[None], ((z - sz) % ngrp, 0, 0))
    return out


def solution(mesh):
    ngrp, ndev = mesh.devices.shape
    ncore = 2
    nx = 4
    ny = ndev // (ncore * nx)
    split = Mesh(mesh.devices.reshape(ngrp, nx, ny, ncore), ("grp", "dx", "dy", "dc"))
    rows = ("dx", "dy", "dc")
    in_specs = (P(None, rows, "grp"), P(None, rows, "grp"), P("grp", rows), P("grp", None), P())
    out_specs = P(None, rows, "grp")
    body = jax.shard_map(shards, mesh=split, in_specs=in_specs, out_specs=out_specs, check_vma=False)
    target = NamedSharding(mesh, P(None, "dev", "grp"))

    def run(*args):
        return lax.with_sharding_constraint(body(*args), target)

    return run
```

```python
import jax
import jax.numpy as jnp
from jax import lax
from jax.sharding import Mesh, NamedSharding, PartitionSpec as P


def apply_update(t_rows, cycle, live, row_gap, col_gap):
    denom = row_gap[:, None] + col_gap[None, :]
    update = jnp.where(live[:, None], cycle / denom, jnp.zeros_like(cycle))
    return t_rows.astype(jnp.float32) + update


def shift(x, axis, step):
    n = lax.axis_size(axis)
    return lax.ppermute(x, axis, [(i, (i + step) % n) for i in range(n)])


def put(buf, piece, base, axis, index):
    start = list(base)
    start[axis] = index
    return lax.dynamic_update_slice(buf, jnp.expand_dims(piece, axis), start)


def hop(piece, ngrp, ncore, sz, sc):
    perm = []
    for i in range(ngrp * ncore):
        gi, ci = divmod(i, ncore)
        perm.append((i, ((gi + sz) % ngrp) * ncore + (ci + sc) % ncore))
    return lax.ppermute(piece, ("grp", "dc"), perm)


def ring4(x, axis, pos, buf, buf_axis, base, near=None):
    from_left = shift(x, axis, 1)
    from_right = shift(x, axis, -1)
    if near is not None:
        near.extend([from_left, from_right])
    half = x.shape[0] // 2
    far_lo = shift(from_left[:half], axis, 1)
    far_hi = shift(from_right[half:], axis, -1)
    buf = put(buf, x, base, buf_axis, pos(0))
    buf = put(buf, from_left, base, buf_axis, pos(-1))
    buf = put(buf, from_right, base, buf_axis, pos(1))
    buf = put(buf, far_lo, base, buf_axis, pos(2))
    hi = list(base)
    inner = buf_axis + 1 if buf_axis == 0 else 0
    hi[inner] = hi[inner] + half
    buf = put(buf, far_hi, hi, buf_axis, pos(2))
    return buf


def shards(packed_w, packed_t, row_energy, col_energy, block_order):
    nx = lax.axis_size("dx")
    ny = lax.axis_size("dy")
    ncore = lax.axis_size("dc")
    ngrp = lax.axis_size("grp")
    x = lax.axis_index("dx")
    y = lax.axis_index("dy")
    c = lax.axis_index("dc")
    z = lax.axis_index("grp")
    rank = (x * ny + y) * ncore + c
    local = packed_t.shape[1]
    ndev = nx * ny * ncore
    true_rows = jnp.arange(local, dtype=jnp.int32) * ndev + rank

    t_rows = lax.all_to_all(packed_t, "grp", split_axis=0, concat_axis=2, tiled=True)[0]
    order = lax.dynamic_index_in_dim(block_order, z, 0, keepdims=False)
    live = true_rows < order
    t_live = jnp.where(live[:, None], t_rows, jnp.zeros_like(t_rows))
    ncol = t_live.shape[1]

    half = local // 2
    by_y = lambda o: (y + o) % ny
    by_x = lambda o: (z - x - o) % nx
    col_a = ring4(t_live[:half], "dy", by_y, jnp.zeros((ny, half, ncol), t_live.dtype), 0, (0, 0, 0))
    row_b = ring4(t_live[half:], "dx", by_x, jnp.zeros((nx, half, ncol), t_live.dtype), 0, (0, 0, 0))
    t_abs = jnp.zeros((nx, ny, local, ncol), t_live.dtype)
    near = []
    t_abs = ring4(col_a, "dx", by_x, t_abs, 0, (0, 0, 0, 0), near)
    t_abs = ring4(row_b, "dy", by_y, t_abs, 1, (0, 0, half, 0), near)

    w_in, _ = lax.optimization_barrier((packed_w, t_live))
    span = packed_w.shape[2] // ny
    cols = span // ncore
    rows_of = []
    for sc in range(ncore):
        chunks = []
        for sz in range(ngrp):
            zt = (z + sz) % ngrp
            ct = (c + sc) % ncore
            piece = jnp.concatenate(
                [lax.dynamic_slice(w_in, (zt, 0, j * span + ct * cols), (1, local, cols))[0]
                 for j in range(ny)], axis=1)
            if sz * 2 == ngrp:
                way = 1 if sc == 0 else -1
                piece = hop(piece, ngrp, ncore, way, sc)
                piece = hop(piece, ngrp, ncore, way, 0)
            elif sz or sc:
                piece = hop(piece, ngrp, ncore, sz, sc)
            chunks.append(piece)
        rows_of.append(jnp.concatenate(chunks, axis=1))
    rows_of, _ = lax.optimization_barrier((rows_of, near))
    w_all = lax.optimization_barrier(jnp.concatenate(rows_of, axis=0))

    t_flat = t_abs.reshape(-1, ncol)
    row_gap = row_energy[0]
    col_gap = col_energy[0]

    width = ncol // ngrp
    out = jnp.zeros((ngrp, local, width), jnp.float32)
    for sz in (2, 1, 3, 0):
        at = ((z + sz) % ngrp) * width
        partial = jnp.dot(w_all, lax.dynamic_slice_in_dim(t_flat, at, width, 1),
                          preferred_element_type=jnp.float32)
        cycle = partial[:local] + shift(partial[local:], "dc", 1)
        piece = apply_update(lax.dynamic_slice_in_dim(t_rows, at, width, 1), cycle, live,
                             row_gap, lax.dynamic_slice_in_dim(col_gap, at, width, 0))
        t_flat, piece = lax.optimization_barrier((t_flat, piece))
        if sz:
            piece = shift(piece, "grp", sz)
        out = lax.dynamic_update_slice(out, piece[None], ((z - sz) % ngrp, 0, 0))
    return out


def solution(mesh):
    ngrp, ndev = mesh.devices.shape
    ncore = 2
    nx = 4
    ny = ndev // (ncore * nx)
    split = Mesh(mesh.devices.reshape(ngrp, nx, ny, ncore), ("grp", "dx", "dy", "dc"))
    rows = ("dx", "dy", "dc")
    in_specs = (P(None, rows, "grp"), P(None, rows, "grp"), P("grp", rows), P("grp", None), P())
    out_specs = P(None, rows, "grp")
    body = jax.shard_map(shards, mesh=split, in_specs=in_specs, out_specs=out_specs, check_vma=False)
    target = NamedSharding(mesh, P(None, "dev", "grp"))

    def run(*args):
        return lax.with_sharding_constraint(body(*args), target)

    return run
```

```python
import jax
import jax.numpy as jnp
from jax import lax
from jax.sharding import Mesh, NamedSharding, PartitionSpec as P


def apply_update(t_rows, cycle, live, row_gap, col_gap):
    denom = row_gap[:, None] + col_gap[None, :]
    update = jnp.where(live[:, None], cycle / denom, jnp.zeros_like(cycle))
    return t_rows.astype(jnp.float32) + update


def shift(x, axis, step):
    n = lax.axis_size(axis)
    return lax.ppermute(x, axis, [(i, (i + step) % n) for i in range(n)])


def put(buf, piece, base, axis, index):
    start = list(base)
    start[axis] = index
    return lax.dynamic_update_slice(buf, jnp.expand_dims(piece, axis), start)


def hop(piece, ngrp, ncore, sz, sc):
    perm = []
    for i in range(ngrp * ncore):
        gi, ci = divmod(i, ncore)
        perm.append((i, ((gi + sz) % ngrp) * ncore + (ci + sc) % ncore))
    return lax.ppermute(piece, ("grp", "dc"), perm)


def ring4(x, axis, pos, buf, buf_axis, base, near=None):
    from_left = shift(x, axis, 1)
    from_right = shift(x, axis, -1)
    if near is not None:
        near.extend([from_left, from_right])
    half = x.shape[0] // 2
    far_lo = shift(from_left[:half], axis, 1)
    far_hi = shift(from_right[half:], axis, -1)
    buf = put(buf, x, base, buf_axis, pos(0))
    buf = put(buf, from_left, base, buf_axis, pos(-1))
    buf = put(buf, from_right, base, buf_axis, pos(1))
    buf = put(buf, far_lo, base, buf_axis, pos(2))
    hi = list(base)
    inner = buf_axis + 1 if buf_axis == 0 else 0
    hi[inner] = hi[inner] + half
    buf = put(buf, far_hi, hi, buf_axis, pos(2))
    return buf


def shards(packed_w, packed_t, row_energy, col_energy, block_order):
    nx = lax.axis_size("dx")
    ny = lax.axis_size("dy")
    ncore = lax.axis_size("dc")
    ngrp = lax.axis_size("grp")
    x = lax.axis_index("dx")
    y = lax.axis_index("dy")
    c = lax.axis_index("dc")
    z = lax.axis_index("grp")
    rank = (x * ny + y) * ncore + c
    local = packed_t.shape[1]
    ndev = nx * ny * ncore
    true_rows = jnp.arange(local, dtype=jnp.int32) * ndev + rank

    width = packed_t.shape[2]
    t_rows = jnp.zeros((local, width * ngrp), packed_t.dtype)
    for sz in range(ngrp):
        piece = lax.dynamic_index_in_dim(packed_t, (z + sz) % ngrp, 0, keepdims=False)
        if sz:
            piece = shift(piece, "grp", sz)
        t_rows = lax.dynamic_update_slice(t_rows, piece, (0, ((z - sz) % ngrp) * width))
    order = lax.dynamic_index_in_dim(block_order, z, 0, keepdims=False)
    live = true_rows < order
    t_live = jnp.where(live[:, None], t_rows, jnp.zeros_like(t_rows))
    ncol = t_live.shape[1]

    half = local // 2
    by_y = lambda o: (y + o) % ny
    by_x = lambda o: (z - x - o) % nx
    col_a = ring4(t_live[:half], "dy", by_y, jnp.zeros((ny, half, ncol), t_live.dtype), 0, (0, 0, 0))
    row_b = ring4(t_live[half:], "dx", by_x, jnp.zeros((nx, half, ncol), t_live.dtype), 0, (0, 0, 0))
    t_abs = jnp.zeros((nx, ny, local, ncol), t_live.dtype)
    near = []
    t_abs = ring4(col_a, "dx", by_x, t_abs, 0, (0, 0, 0, 0), near)
    t_abs = ring4(row_b, "dy", by_y, t_abs, 1, (0, 0, half, 0), near)

    w_in, _ = lax.optimization_barrier((packed_w, t_live))
    span = packed_w.shape[2] // ny
    cols = span // ncore
    rows_of = []
    for sc in range(ncore):
        chunks = []
        for sz in range(ngrp):
            zt = (z + sz) % ngrp
            ct = (c + sc) % ncore
            piece = jnp.concatenate(
                [lax.dynamic_slice(w_in, (zt, 0, j * span + ct * cols), (1, local, cols))[0]
                 for j in range(ny)], axis=1)
            if sz * 2 == ngrp:
                way = 1 if sc == 0 else -1
                piece = hop(piece, ngrp, ncore, way, sc)
                piece = hop(piece, ngrp, ncore, way, 0)
            elif sz or sc:
                piece = hop(piece, ngrp, ncore, sz, sc)
            chunks.append(piece)
        rows_of.append(jnp.concatenate(chunks, axis=1))
    rows_of, _ = lax.optimization_barrier((rows_of, near))
    w_all = lax.optimization_barrier(jnp.concatenate(rows_of, axis=0))

    t_flat = t_abs.reshape(-1, ncol)
    row_gap = row_energy[0]
    col_gap = col_energy[0]

    width = ncol // ngrp
    out = jnp.zeros((ngrp, local, width), jnp.float32)
    for sz in (2, 1, 3, 0):
        at = ((z + sz) % ngrp) * width
        partial = jnp.dot(w_all, lax.dynamic_slice_in_dim(t_flat, at, width, 1),
                          preferred_element_type=jnp.float32)
        cycle = partial[:local] + shift(partial[local:], "dc", 1)
        piece = apply_update(lax.dynamic_slice_in_dim(t_rows, at, width, 1), cycle, live,
                             row_gap, lax.dynamic_slice_in_dim(col_gap, at, width, 0))
        if sz:
            piece = shift(piece, "grp", sz)
        out = lax.dynamic_update_slice(out, piece[None], ((z - sz) % ngrp, 0, 0))
    return out


def solution(mesh):
    ngrp, ndev = mesh.devices.shape
    ncore = 2
    nx = 4
    ny = ndev // (ncore * nx)
    split = Mesh(mesh.devices.reshape(ngrp, nx, ny, ncore), ("grp", "dx", "dy", "dc"))
    rows = ("dx", "dy", "dc")
    in_specs = (P(None, rows, "grp"), P(None, rows, "grp"), P("grp", rows), P("grp", None), P())
    out_specs = P(None, rows, "grp")
    body = jax.shard_map(shards, mesh=split, in_specs=in_specs, out_specs=out_specs, check_vma=False)
    target = NamedSharding(mesh, P(None, "dev", "grp"))

    def run(*args):
        return lax.with_sharding_constraint(body(*args), target)

    return run
```

```python
import jax
import jax.numpy as jnp
from jax import lax
from jax.sharding import Mesh, NamedSharding, PartitionSpec as P


def apply_update(t_rows, cycle, live, row_gap, col_gap):
    denom = row_gap[:, None] + col_gap[None, :]
    update = jnp.where(live[:, None], cycle / denom, jnp.zeros_like(cycle))
    return t_rows.astype(jnp.float32) + update


def shift(x, axis, step):
    n = lax.axis_size(axis)
    return lax.ppermute(x, axis, [(i, (i + step) % n) for i in range(n)])


def put(buf, piece, base, axis, index):
    start = list(base)
    start[axis] = index
    return lax.dynamic_update_slice(buf, jnp.expand_dims(piece, axis), start)


def hop(piece, ngrp, ncore, sz, sc):
    perm = []
    for i in range(ngrp * ncore):
        gi, ci = divmod(i, ncore)
        perm.append((i, ((gi + sz) % ngrp) * ncore + (ci + sc) % ncore))
    return lax.ppermute(piece, ("grp", "dc"), perm)


def ring4(x, axis, pos, buf, buf_axis, base, near=None, direct=False):
    from_left = shift(x, axis, 1)
    from_right = shift(x, axis, -1)
    if near is not None:
        near.extend([from_left, from_right])
    half = x.shape[0] // 2
    if direct:
        far_lo = shift(x[:half], axis, 2)
        far_hi = shift(x[half:], axis, 2)
    else:
        far_lo = shift(from_left[:half], axis, 1)
        far_hi = shift(from_right[half:], axis, -1)
    buf = put(buf, x, base, buf_axis, pos(0))
    buf = put(buf, from_left, base, buf_axis, pos(-1))
    buf = put(buf, from_right, base, buf_axis, pos(1))
    buf = put(buf, far_lo, base, buf_axis, pos(2))
    hi = list(base)
    inner = buf_axis + 1 if buf_axis == 0 else 0
    hi[inner] = hi[inner] + half
    buf = put(buf, far_hi, hi, buf_axis, pos(2))
    return buf


def shards(packed_w, packed_t, row_energy, col_energy, block_order):
    nx = lax.axis_size("dx")
    ny = lax.axis_size("dy")
    ncore = lax.axis_size("dc")
    ngrp = lax.axis_size("grp")
    x = lax.axis_index("dx")
    y = lax.axis_index("dy")
    c = lax.axis_index("dc")
    z = lax.axis_index("grp")
    rank = (x * ny + y) * ncore + c
    local = packed_t.shape[1]
    ndev = nx * ny * ncore
    true_rows = jnp.arange(local, dtype=jnp.int32) * ndev + rank

    width = packed_t.shape[2]
    t_rows = jnp.zeros((local, width * ngrp), packed_t.dtype)
    for sz in range(ngrp):
        piece = lax.dynamic_index_in_dim(packed_t, (z + sz) % ngrp, 0, keepdims=False)
        if sz:
            piece = shift(piece, "grp", sz)
        t_rows = lax.dynamic_update_slice(t_rows, piece, (0, ((z - sz) % ngrp) * width))
    order = lax.dynamic_index_in_dim(block_order, z, 0, keepdims=False)
    live = true_rows < order
    t_live = jnp.where(live[:, None], t_rows, jnp.zeros_like(t_rows))
    ncol = t_live.shape[1]

    half = local // 2
    by_y = lambda o: (y + o) % ny
    by_x = lambda o: (z - x - o) % nx
    col_a = ring4(t_live[:half], "dy", by_y, jnp.zeros((ny, half, ncol), t_live.dtype), 0, (0, 0, 0),
                  direct=True)
    row_b = ring4(t_live[half:], "dx", by_x, jnp.zeros((nx, half, ncol), t_live.dtype), 0, (0, 0, 0),
                  direct=True)
    t_abs = jnp.zeros((nx, ny, local, ncol), t_live.dtype)
    near = []
    t_abs = ring4(col_a, "dx", by_x, t_abs, 0, (0, 0, 0, 0), near)
    t_abs = ring4(row_b, "dy", by_y, t_abs, 1, (0, 0, half, 0), near)

    w_in, _ = lax.optimization_barrier((packed_w, t_live))
    span = packed_w.shape[2] // ny
    cols = span // ncore
    rows_of = []
    for sc in range(ncore):
        chunks = []
        for sz in range(ngrp):
            zt = (z + sz) % ngrp
            ct = (c + sc) % ncore
            piece = jnp.concatenate(
                [lax.dynamic_slice(w_in, (zt, 0, j * span + ct * cols), (1, local, cols))[0]
                 for j in range(ny)], axis=1)
            if sz * 2 == ngrp:
                way = 1 if sc == 0 else -1
                piece = hop(piece, ngrp, ncore, way, sc)
                piece = hop(piece, ngrp, ncore, way, 0)
            elif sz or sc:
                piece = hop(piece, ngrp, ncore, sz, sc)
            chunks.append(piece)
        rows_of.append(jnp.concatenate(chunks, axis=1))
    rows_of, _ = lax.optimization_barrier((rows_of, near))
    w_all = lax.optimization_barrier(jnp.concatenate(rows_of, axis=0))

    t_flat = t_abs.reshape(-1, ncol)
    row_gap = row_energy[0]
    col_gap = col_energy[0]

    width = ncol // ngrp
    out = jnp.zeros((ngrp, local, width), jnp.float32)
    for sz in (2, 1, 3, 0):
        at = ((z + sz) % ngrp) * width
        partial = jnp.dot(w_all, lax.dynamic_slice_in_dim(t_flat, at, width, 1),
                          preferred_element_type=jnp.float32)
        cycle = partial[:local] + shift(partial[local:], "dc", 1)
        piece = apply_update(lax.dynamic_slice_in_dim(t_rows, at, width, 1), cycle, live,
                             row_gap, lax.dynamic_slice_in_dim(col_gap, at, width, 0))
        if sz:
            piece = shift(piece, "grp", sz)
        out = lax.dynamic_update_slice(out, piece[None], ((z - sz) % ngrp, 0, 0))
    return out


def solution(mesh):
    ngrp, ndev = mesh.devices.shape
    ncore = 2
    nx = 4
    ny = ndev // (ncore * nx)
    split = Mesh(mesh.devices.reshape(ngrp, nx, ny, ncore), ("grp", "dx", "dy", "dc"))
    rows = ("dx", "dy", "dc")
    in_specs = (P(None, rows, "grp"), P(None, rows, "grp"), P("grp", rows), P("grp", None), P())
    out_specs = P(None, rows, "grp")
    body = jax.shard_map(shards, mesh=split, in_specs=in_specs, out_specs=out_specs, check_vma=False)
    target = NamedSharding(mesh, P(None, "dev", "grp"))

    def run(*args):
        return lax.with_sharding_constraint(body(*args), target)

    return run
```

```python
import jax
import jax.numpy as jnp
from jax import lax
from jax.sharding import Mesh, NamedSharding, PartitionSpec as P


def apply_update(t_rows, cycle, live, row_gap, col_gap):
    denom = row_gap[:, None] + col_gap[None, :]
    update = jnp.where(live[:, None], cycle / denom, jnp.zeros_like(cycle))
    return t_rows.astype(jnp.float32) + update


def shift(x, axis, step):
    n = lax.axis_size(axis)
    return lax.ppermute(x, axis, [(i, (i + step) % n) for i in range(n)])


def put(buf, piece, base, axis, index):
    start = list(base)
    start[axis] = index
    return lax.dynamic_update_slice(buf, jnp.expand_dims(piece, axis), start)


def hop(piece, ngrp, ncore, sz, sc):
    perm = []
    for i in range(ngrp * ncore):
        gi, ci = divmod(i, ncore)
        perm.append((i, ((gi + sz) % ngrp) * ncore + (ci + sc) % ncore))
    return lax.ppermute(piece, ("grp", "dc"), perm)


def ring4(x, axis, pos, buf, buf_axis, base, near=None):
    from_left = shift(x, axis, 1)
    from_right = shift(x, axis, -1)
    if near is not None:
        near.extend([from_left, from_right])
    half = x.shape[0] // 2
    far_lo = shift(from_left[:half], axis, 1)
    far_hi = shift(from_right[half:], axis, -1)
    buf = put(buf, x, base, buf_axis, pos(0))
    buf = put(buf, from_left, base, buf_axis, pos(-1))
    buf = put(buf, from_right, base, buf_axis, pos(1))
    buf = put(buf, far_lo, base, buf_axis, pos(2))
    hi = list(base)
    inner = buf_axis + 1 if buf_axis == 0 else 0
    hi[inner] = hi[inner] + half
    buf = put(buf, far_hi, hi, buf_axis, pos(2))
    return buf


def shards(packed_w, packed_t, row_energy, col_energy, block_order):
    nx = lax.axis_size("dx")
    ny = lax.axis_size("dy")
    ncore = lax.axis_size("dc")
    ngrp = lax.axis_size("grp")
    x = lax.axis_index("dx")
    y = lax.axis_index("dy")
    c = lax.axis_index("dc")
    z = lax.axis_index("grp")
    rank = (x * ny + y) * ncore + c
    local = packed_t.shape[1]
    ndev = nx * ny * ncore
    true_rows = jnp.arange(local, dtype=jnp.int32) * ndev + rank

    width = packed_t.shape[2]
    t_rows = jnp.zeros((local, width * ngrp), packed_t.dtype)
    for sz in range(ngrp):
        piece = lax.dynamic_index_in_dim(packed_t, (z + sz) % ngrp, 0, keepdims=False)
        if sz:
            piece = shift(piece, "grp", sz)
        t_rows = lax.dynamic_update_slice(t_rows, piece, (0, ((z - sz) % ngrp) * width))
    order = lax.dynamic_index_in_dim(block_order, z, 0, keepdims=False)
    live = true_rows < order
    t_live = jnp.where(live[:, None], t_rows, jnp.zeros_like(t_rows))
    ncol = t_live.shape[1]

    half = local // 2
    by_y = lambda o: (y + o) % ny
    by_x = lambda o: (z - x - o) % nx
    col_a = ring4(t_live[:half], "dy", by_y, jnp.zeros((ny, half, ncol), t_live.dtype), 0, (0, 0, 0))
    row_b = ring4(t_live[half:], "dx", by_x, jnp.zeros((nx, half, ncol), t_live.dtype), 0, (0, 0, 0))
    t_abs = jnp.zeros((nx, ny, local, ncol), t_live.dtype)
    near = []
    t_abs = ring4(col_a, "dx", by_x, t_abs, 0, (0, 0, 0, 0), near)
    t_abs = ring4(row_b, "dy", by_y, t_abs, 1, (0, 0, half, 0), near)

    w_in, _ = lax.optimization_barrier((packed_w, t_live))
    span = packed_w.shape[2] // ny
    cols = span // ncore
    rows_of = []
    for sc in range(ncore):
        chunks = []
        for sz in range(ngrp):
            zt = (z + sz) % ngrp
            ct = (c + sc) % ncore
            piece = jnp.concatenate(
                [lax.dynamic_slice(w_in, (zt, 0, j * span + ct * cols), (1, local, cols))[0]
                 for j in range(ny)], axis=1)
            if sz or sc:
                piece = hop(piece, ngrp, ncore, sz, sc)
            chunks.append(piece)
        rows_of.append(jnp.concatenate(chunks, axis=1))
    rows_of, _ = lax.optimization_barrier((rows_of, near))
    w_all = lax.optimization_barrier(jnp.concatenate(rows_of, axis=0))

    t_flat = t_abs.reshape(-1, ncol)
    row_gap = row_energy[0]
    col_gap = col_energy[0]

    width = ncol // ngrp
    out = jnp.zeros((ngrp, local, width), jnp.float32)
    for sz in (2, 1, 3, 0):
        at = ((z + sz) % ngrp) * width
        partial = jnp.dot(w_all, lax.dynamic_slice_in_dim(t_flat, at, width, 1),
                          preferred_element_type=jnp.float32)
        cycle = partial[:local] + shift(partial[local:], "dc", 1)
        piece = apply_update(lax.dynamic_slice_in_dim(t_rows, at, width, 1), cycle, live,
                             row_gap, lax.dynamic_slice_in_dim(col_gap, at, width, 0))
        if sz:
            piece = shift(piece, "grp", sz)
        out = lax.dynamic_update_slice(out, piece[None], ((z - sz) % ngrp, 0, 0))
    return out


def solution(mesh):
    ngrp, ndev = mesh.devices.shape
    ncore = 2
    nx = 4
    ny = ndev // (ncore * nx)
    split = Mesh(mesh.devices.reshape(ngrp, nx, ny, ncore), ("grp", "dx", "dy", "dc"))
    rows = ("dx", "dy", "dc")
    in_specs = (P(None, rows, "grp"), P(None, rows, "grp"), P("grp", rows), P("grp", None), P())
    out_specs = P(None, rows, "grp")
    body = jax.shard_map(shards, mesh=split, in_specs=in_specs, out_specs=out_specs, check_vma=False)
    target = NamedSharding(mesh, P(None, "dev", "grp"))

    def run(*args):
        return lax.with_sharding_constraint(body(*args), target)

    return run
```
